128 devices in a mesh: tok: 16 (over x, z), row: 4 (over y), col: 2 (over core).
Axes of the slice: x: 4, y: 4, z: 4, core: 2. Of those that a mesh axis runs over, the one named last changes fastest.
Arguments:
- block_input_rows: bfloat16 [8192, 4096], P(('tok', 'row'), 'col'), may hold values from -18 to 18
- input_norm_scale: bfloat16 [4096], P('col'), may hold values from 0.6 to 10, as said below
- query_key_value_weight: bfloat16 [4096, 16, 3, 128], P('col', 'row'), may hold values from -0.09375 to 0.09375
- adapter_down_weight: bfloat16 [4096, 128], P('col'), may hold values from -0.09375 to 0.09375
- adapter_up_weight: bfloat16 [128, 16, 3, 128], P(None, 'row'), may hold values from -0.5 to 0.5
- output_projection_weight: bfloat16 [2048, 2048], P(('row', 'col')), may hold values from -0.125 to 0.125
- prompt_segment_index: int32 [8192], replicated, may hold values from 0 to 3, never falling along the last dimension, each value on 1 to 4352 neighbouring positions
- cache_owner_index: int32 [8192, 1], P('tok'), may hold values from 0 to 15; in each aligned block of 512 rows (0 to 511, 512 to 1023, ...) at most 64 rows name the same one
Outputs:
- block_output: bfloat16 [8192, 2048], P(('tok', 'row', 'col'))
- kv_cache: bfloat16 [16384, 16, 2, 128], P('tok', ('row', 'col'))
The draws below stay inside these ranges and needn't reach their ends.
Inputs may be any that keep to these rules, and one draw needn't show every extreme that they name: `prompt_segment_index`: never falls along the tokens; every prompt holds 1 to 4352 tokens and one holds exactly 4352. `cache_owner_index`: in each aligned block of 512 tokens no owner is named by more than 64 tokens; some owner is named exactly 64 times in some block. `input_norm_scale`: positive gains.
All inputs are finite; a program needn't handle non-finite values.
Results may differ from the reference program's by a relative error of at most 0.015.
The reference program's roundings to bfloat16 on the way count: a program that leaves them out, or rounds other values in their place, can miss the bound.
Values may be sent and summed in bfloat16 or wider, within the bound.
No kernel may reach another device: no remote copies, remote signals or barrier semaphores. Data moves between devices by JAX's collectives and lax.ppermute only.
A program may use at most 192 MiB of HBM per device.

```python
import math
import jax
import jax.numpy as jnp
import numpy as np
from jax import lax

INPUT_WIDTH = 4096
DOUT = 2048
HEAD_SIZE = 128
ADAPTER_RANK = 128
LOCAL_HEADS = 16
TOK_DEV = 512
SEGS = 4
TOKENS = 8192
MAXLEN = 4352
CAP = 64
CACHE_SLOTS = 16384
N_TOK = 16


def draw_block_input_rows(key, part):
    first = jax.random.fold_in(key, 0)
    columns = jnp.where(jnp.arange(INPUT_WIDTH) < INPUT_WIDTH // 2, 1.0, 0.4).astype(jnp.float32)
    values = jnp.clip(jax.random.normal(first, (TOKENS, INPUT_WIDTH), jnp.float32), -6.0, 6.0) * columns[None, :]
    return values.astype(jnp.bfloat16)


def draw_input_norm_scale(key, part):
    gains = jnp.exp(jax.random.uniform(key, (INPUT_WIDTH,), jnp.float32, -0.5, 0.45))
    return gains.astype(jnp.bfloat16)


def block_scale(stream_key, dims, cuts, low, top_value):
    loudness = 1.0
    for dim, shards_of in cuts:
        steps = jax.random.uniform(jax.random.fold_in(jax.random.fold_in(stream_key, 6), dim), (shards_of,), jnp.float32, low / len(cuts), top_value / len(cuts))
        loudness = loudness * jnp.repeat(jnp.exp(steps), dims[dim] // shards_of).reshape((-1,) + (1,) * (len(dims) - 1 - dim))
    return loudness


def split_up(number_of, total, reach, slope):
    loads = [(1 << 20) // math.isqrt(standing ** slope) + 1 for standing in range(2, number_of + 1)]
    surplus, given = total - reach - (number_of - 1), [1] * (number_of - 1)
    while surplus > 0:
        free = [i for i in range(number_of - 1) if given[i] < reach]
        whole, left = sum([loads[i] for i in free]), surplus
        for i in free:
            more = min(reach - given[i], max(1, left * loads[i] // whole), surplus)
            given[i] = given[i] + more
            surplus = surplus - more
    return np.array([reach] + given)


def ragged(stream_key, amount, total, bound, slope):
    if amount == 2:
        one = jax.random.randint(stream_key, (), max(1, total - bound), min(bound, total - 1) + 1)
        return jnp.stack([one, total - one])
    lengths = jnp.asarray(split_up(amount, total, bound, slope), jnp.int32)
    twos = (amount - 1) // 2
    source_of, receiver = lengths[1:1 + 2 * twos:2], lengths[2:2 + 2 * twos:2]
    room = jnp.minimum(source_of - 1, bound - receiver)
    passed = jax.random.randint(jax.random.fold_in(stream_key, 1), (twos,), 0, 1 << 20) % (room + 1)
    lengths = lengths.at[1:1 + 2 * twos:2].set(source_of - passed).at[2:2 + 2 * twos:2].set(receiver + passed)
    return lengths[jax.random.permutation(jax.random.fold_in(stream_key, 2), amount)]


def assign_block(stream_key, own, number, rows, amount, top, most, slope):
    sequence = jax.random.permutation(stream_key, amount)
    heavy_load, usual = load_shares(amount, rows * top, most, slope, True), load_shares(amount, rows * top, most, slope, False)
    places = jnp.arange(amount)

    def named(lengths, rotation):
        used = int((lengths > 0).sum())
        fixed = max(1, used // 4)
        moved = fixed + (places - fixed + rotation * (used - fixed)) % max(1, amount - fixed)
        return jnp.zeros((amount,), jnp.int32).at[sequence[jnp.where(places < fixed, places, moved)]].set(jnp.asarray(lengths, jnp.int32))

    lengths = jnp.where(number % 4 == 0, named(heavy_load, number // 4), named(usual, number - number // 4 - 1))
    mixed = jax.random.permutation(jax.random.fold_in(own, 3), amount)
    donor, sink = mixed[0:amount // 2 * 2:2], mixed[1:amount // 2 * 2:2]
    room = jnp.minimum(lengths[donor] - 1, most - lengths[sink]) // 2
    room = jnp.where((donor == sequence[0]) | (sink == sequence[0]) | (lengths[sink] == 0), 0, jnp.maximum(room, 0))
    moved = jax.random.randint(jax.random.fold_in(own, 4), (amount // 2,), 0, 1 << 20) % (room + 1)
    lengths = lengths.at[donor].add(-moved).at[sink].add(moved)
    members = jnp.searchsorted(jnp.cumsum(lengths), jnp.arange(rows * top), side="right").astype(jnp.int32)
    grid = members.reshape(top, rows).T
    grid = grid[jax.random.permutation(jax.random.fold_in(own, 1), rows)]
    rotation = jax.random.randint(jax.random.fold_in(own, 2), (rows, 1), 0, top)
    return jnp.take_along_axis(grid, (jnp.arange(top)[None, :] + rotation) % top, axis=1)


def load_shares(count, total, most, slope, full):
    portions = [(1 << 20) // math.isqrt(standing ** slope) + 1 for standing in range(1, count + 1)]
    largest = most if full else min(most, max(-(-total // count), total * portions[0] // sum(portions)))
    least = 1 if total - largest >= count - 1 else 0
    given, rest = [largest] + [least] * (count - 1), total - largest - least * (count - 1)
    while rest > 0:
        free = [i for i in range(1, count) if given[i] < largest] or [i for i in range(1, count) if given[i] < most]
        whole, left = sum([portions[i] for i in free]), rest
        for i in free:
            extra = min(most - given[i], max(1, left * portions[i] // whole), rest)
            given[i] = given[i] + extra
            rest = rest - extra
    return np.array(given)


def noise(rng, shape, scale, reach, shards=(), held_as=jnp.bfloat16):
    drawn = jax.random.normal(rng, shape, jnp.float32) * scale
    if len(shards) > 0:
        drawn = block_scale(rng, shape, shards, -0.22, 0.18) * drawn
    return jnp.clip(drawn, min=-reach, max=reach).astype(held_as)


def setup_inputs(seed: int = 0) -> dict:
    key_list = jax.random.split(jax.random.key(seed), 9)
    block_input_rows = draw_block_input_rows(jax.random.fold_in(key_list[8], 71), 0)
    input_norm_scale = draw_input_norm_scale(jax.random.fold_in(key_list[8], 71), 0)
    query_key_value_weight = noise(key_list[2], (INPUT_WIDTH, LOCAL_HEADS, 3, HEAD_SIZE), INPUT_WIDTH ** -0.5, 0.09375, ((0, 2), (1, 4)))
    adapter_down_weight = noise(key_list[3], (INPUT_WIDTH, ADAPTER_RANK), INPUT_WIDTH ** -0.5, 0.09375, ((0, 2),))
    adapter_up_weight = noise(key_list[4], (ADAPTER_RANK, LOCAL_HEADS, 3, HEAD_SIZE), ADAPTER_RANK ** -0.5, 0.5, ((1, 4),))
    output_projection_weight = noise(key_list[5], (LOCAL_HEADS * HEAD_SIZE, DOUT), (LOCAL_HEADS * HEAD_SIZE) ** -0.5, 0.125, ((0, 8),))
    prompt_segment_index = jnp.searchsorted(jnp.cumsum(ragged(key_list[6], SEGS, TOKENS, MAXLEN, 2)), jnp.arange(TOKENS), side="right").astype(jnp.int32)
    cache_owner_index_keys = jax.random.split(jax.random.fold_in(key_list[7], 1), TOKENS // TOK_DEV)
    cache_owner_index_turns = jax.random.permutation(jax.random.fold_in(key_list[7], 3), TOKENS // TOK_DEV)
    cache_owner_index = jax.vmap(lambda own, number: assign_block(jax.random.fold_in(key_list[7], 2), own, number, TOK_DEV, N_TOK, 1, CAP, 2))(cache_owner_index_keys, cache_owner_index_turns).reshape((TOKENS, 1))
    return {"block_input_rows": block_input_rows, "input_norm_scale": input_norm_scale, "query_key_value_weight": query_key_value_weight, "adapter_down_weight": adapter_down_weight, "adapter_up_weight": adapter_up_weight, "output_projection_weight": output_projection_weight, "prompt_segment_index": prompt_segment_index, "cache_owner_index": cache_owner_index}


def reference(block_input_rows, input_norm_scale, query_key_value_weight, adapter_down_weight, adapter_up_weight, output_projection_weight, prompt_segment_index, cache_owner_index):
    wide = block_input_rows.astype(jnp.float32)
    mean_sq = lax.optimization_barrier(jnp.mean(wide * wide, axis=1, keepdims=True))
    normalized_input = (wide * lax.rsqrt(mean_sq + 1e-06) * input_norm_scale.astype(jnp.float32)[None, :]).astype(jnp.bfloat16)
    main = jnp.dot(normalized_input, query_key_value_weight.reshape(INPUT_WIDTH, LOCAL_HEADS * 3 * HEAD_SIZE), preferred_element_type=jnp.float32)
    adapter_hidden = jnp.dot(normalized_input, adapter_down_weight, preferred_element_type=jnp.float32)
    adapter_down_output = jnp.dot(adapter_hidden, adapter_up_weight.astype(jnp.float32).reshape(ADAPTER_RANK, LOCAL_HEADS * 3 * HEAD_SIZE), precision=lax.Precision.HIGHEST)
    qkv = (main + adapter_down_output).astype(jnp.bfloat16).reshape(TOKENS, LOCAL_HEADS, 3, HEAD_SIZE)
    query = jnp.transpose(qkv[:, :, 0], (1, 0, 2))
    keys = jnp.transpose(qkv[:, :, 1], (1, 0, 2))
    values = jnp.transpose(qkv[:, :, 2], (1, 0, 2))
    position = jnp.arange(TOKENS, dtype=jnp.int32)
    allowed = (prompt_segment_index[:, None] == prompt_segment_index[None, :]) & (position[None, :] <= position[:, None])
    scale = 1.0 / HEAD_SIZE ** 0.5

    def one_head(inputs):
        head_q, head_k, head_v = inputs
        score = jnp.dot(head_q, head_k.T, preferred_element_type=jnp.float32) * scale
        masked = jnp.where(allowed, score, -1e+30)
        top = lax.optimization_barrier(jnp.max(masked, axis=1, keepdims=True))
        weights = jnp.where(allowed, jnp.exp(score - top), 0.0).astype(jnp.bfloat16)
        total = lax.optimization_barrier(jnp.sum(weights.astype(jnp.float32), axis=1, keepdims=True))
        summed = jnp.dot(weights, head_v, preferred_element_type=jnp.float32)
        return (summed / total).astype(jnp.bfloat16)
    attended = lax.map(one_head, (query, keys, values))
    attended = jnp.transpose(attended, (1, 0, 2)).reshape(TOKENS, LOCAL_HEADS * HEAD_SIZE)
    block_output = jnp.dot(attended, output_projection_weight, preferred_element_type=jnp.float32).astype(jnp.bfloat16)
    owner = cache_owner_index[:, 0]
    onehot = (owner[:, None] == jnp.arange(N_TOK, dtype=jnp.int32)[None, :]).astype(jnp.int32)
    onehot = onehot.reshape(N_TOK, TOK_DEV, N_TOK)
    before = jnp.cumsum(onehot, axis=1) - onehot
    rank = lax.optimization_barrier(jnp.sum(before * onehot, axis=2)).reshape(TOKENS)
    source = position // TOK_DEV
    slot = (owner * (N_TOK * CAP) + source * CAP + rank).astype(jnp.int32)
    pairs = jnp.stack([qkv[:, :, 1], qkv[:, :, 2]], axis=2)
    kv_cache = jnp.zeros((CACHE_SLOTS, LOCAL_HEADS, 2, HEAD_SIZE), jnp.bfloat16).at[slot].set(pairs)
    return (block_output, kv_cache)
```

```python
import jax
import jax.numpy as jnp
from jax import lax
from jax.sharding import PartitionSpec as P


INPUT_WIDTH = 4096
HEAD_SIZE = 128
ADAPTER_RANK = 128
MAXLEN = 4352


def fold_piece(carry, piece, query, own_seg, own_start, prompt_segment_index, scale):
    top_old, _, _ = carry
    count = piece.shape[0]
    key_pos = jnp.arange(count, dtype=jnp.int32)
    query_pos = own_start + jnp.arange(query.shape[1], dtype=jnp.int32)
    allowed = (
        (own_seg[:, None] == prompt_segment_index[None, :])
        & (key_pos[None, :] <= query_pos[:, None])
        & (key_pos[None, :] >= 0)
    )
    score = (
        jnp.einsum("htd,shd->hts", query, piece[:, :, 0], preferred_element_type=jnp.float32)
        * scale
    )
    masked = jnp.where(allowed[None], score, -1e30)
    top_new = jnp.maximum(top_old, jnp.max(masked, axis=2))
    weights = jnp.where(allowed[None], jnp.exp(score - top_new[:, :, None]), 0.0).astype(
        jnp.bfloat16
    )
    total_new = jnp.sum(weights.astype(jnp.float32), axis=2)
    acc_new = jnp.einsum(
        "hts,shd->htd", weights, piece[:, :, 1], preferred_element_type=jnp.float32
    )
    return (top_new, total_new, acc_new)


def shards_body(
    block_input_rows,
    input_norm_scale,
    query_key_value_weight,
    adapter_down_weight,
    adapter_up_weight,
    output_projection_weight,
    prompt_segment_index,
    cache_owner_index,
):
    gathered = lax.all_gather(block_input_rows, "row", axis=0, tiled=True)
    wide = gathered.astype(jnp.float32)
    partial_sq = jnp.sum(wide * wide, axis=1)
    total_sq = lax.psum(partial_sq, "col")
    inverse = lax.rsqrt(total_sq / INPUT_WIDTH + 1e-06)
    normalized_input = (
        wide * inverse[:, None] * input_norm_scale.astype(jnp.float32)[None, :]
    ).astype(jnp.bfloat16)
    adapter_hidden = jnp.dot(
        normalized_input, adapter_down_weight, preferred_element_type=jnp.float32
    )
    tok_dev = gathered.shape[0]
    local_head_count = query_key_value_weight.shape[1]
    flat_weight = query_key_value_weight.reshape(
        query_key_value_weight.shape[0], local_head_count, 3 * HEAD_SIZE
    )
    flattened_up_weight = adapter_up_weight.reshape(ADAPTER_RANK, local_head_count, 3 * HEAD_SIZE)
    heads_dev = local_head_count // lax.axis_size("col")
    main = jnp.einsum(
        "td,dhe->hte", normalized_input, flat_weight, preferred_element_type=jnp.float32
    )
    adapter_down_output = jnp.einsum(
        "tr,rhe->hte",
        adapter_hidden,
        flattened_up_weight.astype(jnp.float32),
        precision=lax.Precision.HIGHEST,
    )
    mixed = lax.psum_scatter(main + adapter_down_output, "col", scatter_dimension=0, tiled=True)
    qkv = mixed.astype(jnp.bfloat16).reshape(heads_dev, tok_dev, 3, HEAD_SIZE)
    query = qkv[:, :, 0]
    kv_tok = jnp.transpose(qkv[:, :, 1:3], (1, 0, 2, 3))
    count_tok = lax.axis_size("tok")
    me = lax.axis_index("tok")
    own_start = me * tok_dev
    own_seg = lax.dynamic_slice_in_dim(prompt_segment_index, own_start, tok_dev, 0)
    scale = 1.0 / HEAD_SIZE**0.5
    back = min(count_tok - 1, -(-(MAXLEN - 1) // tok_dev))
    window = (back + 1) * tok_dev
    first = jnp.clip(me - back, 0, count_tok - 1 - back) * tok_dev
    gathered_kv = lax.all_gather(kv_tok, "tok", axis=0, tiled=True)
    piece = lax.dynamic_slice_in_dim(gathered_kv, first, window, 0)
    key_seg = lax.dynamic_slice_in_dim(prompt_segment_index, first, window, 0)
    init = (
        jnp.full((heads_dev, tok_dev), -1e30, jnp.float32),
        jnp.zeros((heads_dev, tok_dev), jnp.float32),
        jnp.zeros((heads_dev, tok_dev, HEAD_SIZE), jnp.float32),
    )
    state = fold_piece(init, piece, query, own_seg, own_start - first, key_seg, scale)
    attended = (state[2] / state[1][:, :, None]).astype(jnp.bfloat16)
    attended = jnp.transpose(attended, (1, 0, 2)).reshape(tok_dev, heads_dev * HEAD_SIZE)
    block_output = lax.psum_scatter(
        jnp.dot(attended, output_projection_weight, preferred_element_type=jnp.float32).astype(
            jnp.bfloat16
        ),
        ("row", "col"),
        scatter_dimension=0,
        tiled=True,
    )
    capacity = max(2, 2 * tok_dev // count_tok)
    owner = cache_owner_index[:, 0]
    onehot = (owner[:, None] == jnp.arange(count_tok, dtype=jnp.int32)[None, :]).astype(jnp.int32)
    before = jnp.cumsum(onehot, axis=0) - onehot
    rank = jnp.sum(before * onehot, axis=1)
    slot = ((owner - me) % count_tok) * capacity + rank
    selector = (jnp.arange(count_tok * capacity, dtype=jnp.int32)[:, None] == slot[None, :]).astype(
        jnp.bfloat16
    )
    outgoing = jnp.dot(
        selector,
        kv_tok.reshape(tok_dev, heads_dev * 2 * HEAD_SIZE),
        preferred_element_type=jnp.float32,
    ).astype(jnp.bfloat16).reshape(count_tok, capacity, heads_dev * 2 * HEAD_SIZE)
    chunks = [outgoing[0]]
    for shift in range(1, count_tok):
        pairs = [(j, (j + shift) % count_tok) for j in range(count_tok)]
        chunks.append(lax.ppermute(outgoing[shift], "tok", pairs))
    arrived = jnp.stack(chunks)
    received = jnp.take(arrived, (me - jnp.arange(count_tok)) % count_tok, axis=0)
    kv_cache = received.reshape(count_tok * capacity, heads_dev, 2, HEAD_SIZE)
    return (block_output, kv_cache)


def solution(mesh):
    placed = (
        P(("tok", "row"), "col"),
        P("col"),
        P("col", "row", None, None),
        P("col", None),
        P(None, "row", None, None),
        P(("row", "col"), None),
        P(),
        P("tok", None),
    )
    return jax.shard_map(
        shards_body,
        mesh=mesh,
        in_specs=placed,
        out_specs=(P(("tok", "row", "col"), None), P("tok", ("row", "col"), None, None)),
        check_vma=False,
    )
```

```python
import jax
import jax.numpy as jnp
from jax import lax
from jax.sharding import PartitionSpec as P


INPUT_WIDTH = 4096
HEAD_SIZE = 128
ADAPTER_RANK = 128
MAXLEN = 4352

def fold_piece(carry, piece, query, own_seg, own_start, prompt_segment_index, scale):
    top_old, _, _ = carry
    count = piece.shape[0]
    key_pos = jnp.arange(count, dtype=jnp.int32)
    query_pos = own_start + jnp.arange(query.shape[1], dtype=jnp.int32)
    allowed = (
        (own_seg[:, None] == prompt_segment_index[None, :])
        & (key_pos[None, :] <= query_pos[:, None])
        & (key_pos[None, :] >= 0)
    )
    score = (
        jnp.einsum("htd,shd->hts", query, piece[:, :, 0], preferred_element_type=jnp.float32)
        * scale
    )
    masked = jnp.where(allowed[None], score, -1e30)
    top_new = jnp.maximum(top_old, jnp.max(masked, axis=2))
    weights = jnp.where(allowed[None], jnp.exp(score - top_new[:, :, None]), 0.0).astype(
        jnp.bfloat16
    )
    total_new = jnp.sum(weights.astype(jnp.float32), axis=2)
    acc_new = jnp.einsum(
        "hts,shd->htd", weights, piece[:, :, 1], preferred_element_type=jnp.float32
    )
    return (top_new, total_new, acc_new)

def shards_body(
    block_input_rows,
    input_norm_scale,
    query_key_value_weight,
    adapter_down_weight,
    adapter_up_weight,
    output_projection_weight,
    prompt_segment_index,
    cache_owner_index,
):
    gathered = lax.all_gather(block_input_rows, "row", axis=0, tiled=True)
    wide = gathered.astype(jnp.float32)
    partial_sq = jnp.sum(wide * wide, axis=1)
    total_sq = lax.psum(partial_sq, "col")
    inverse = lax.rsqrt(total_sq / INPUT_WIDTH + 1e-06)
    normalized_input = (
        wide * inverse[:, None] * input_norm_scale.astype(jnp.float32)[None, :]
    ).astype(jnp.bfloat16)
    adapter_hidden = jnp.dot(
        normalized_input, adapter_down_weight, preferred_element_type=jnp.float32
    )
    tok_dev = gathered.shape[0]
    local_head_count = query_key_value_weight.shape[1]
    flat_weight = query_key_value_weight.reshape(
        query_key_value_weight.shape[0], local_head_count, 3 * HEAD_SIZE
    )
    flattened_up_weight = adapter_up_weight.reshape(ADAPTER_RANK, local_head_count, 3 * HEAD_SIZE)
    heads_dev = local_head_count // lax.axis_size("col")
    main = jnp.einsum(
        "td,dhe->hte", normalized_input, flat_weight, preferred_element_type=jnp.float32
    )
    adapter_down_output = jnp.einsum(
        "tr,rhe->hte",
        adapter_hidden,
        flattened_up_weight.astype(jnp.float32),
        precision=lax.Precision.HIGHEST,
    )
    mixed = lax.psum_scatter(main + adapter_down_output, "col", scatter_dimension=0, tiled=True)
    qkv = mixed.astype(jnp.bfloat16).reshape(heads_dev, tok_dev, 3, HEAD_SIZE)
    query = qkv[:, :, 0]
    kv_tok = jnp.transpose(qkv[:, :, 1:3], (1, 0, 2, 3))
    count_tok = lax.axis_size("tok")
    me = lax.axis_index("tok")
    own_start = me * tok_dev
    own_seg = lax.dynamic_slice_in_dim(prompt_segment_index, own_start, tok_dev, 0)
    scale = 1.0 / HEAD_SIZE**0.5
    back = min(count_tok - 1, -(-(MAXLEN - 1) // tok_dev))
    window = (back + 1) * tok_dev
    first = jnp.clip(me - back, 0, count_tok - 1 - back) * tok_dev
    key_seg = lax.dynamic_slice_in_dim(prompt_segment_index, first, window, 0)
    init = (
        jnp.full((1, tok_dev), -1e30, jnp.float32),
        jnp.zeros((1, tok_dev), jnp.float32),
        jnp.zeros((1, tok_dev, HEAD_SIZE), jnp.float32),
    )
    capacity = max(2, 2 * tok_dev // count_tok)
    owner = cache_owner_index[:, 0]
    onehot = (owner[:, None] == jnp.arange(count_tok, dtype=jnp.int32)[None, :]).astype(jnp.int32)
    before = jnp.cumsum(onehot, axis=0) - onehot
    rank = jnp.sum(before * onehot, axis=1)
    slot = owner * capacity + rank
    selector = (jnp.arange(count_tok * capacity, dtype=jnp.int32)[:, None] == slot[None, :]).astype(
        jnp.bfloat16
    )
    outgoing = jnp.dot(
        selector,
        kv_tok.reshape(tok_dev, heads_dev * 2 * HEAD_SIZE),
        preferred_element_type=jnp.float32,
    ).astype(jnp.bfloat16).reshape(count_tok, capacity, heads_dev * 2 * HEAD_SIZE)
    gathered = []
    for head in range(heads_dev):
        gathered.append(lax.all_gather(kv_tok[:, head : head + 1], "tok", axis=0, tiled=True))
    received = lax.all_to_all(outgoing, "tok", split_axis=0, concat_axis=0, tiled=True)
    received, gathered[0] = lax.optimization_barrier((received, gathered[0]))
    states = []
    for head in range(heads_dev):
        gathered_kv = gathered[head]
        if head > 0:
            gathered_kv, _ = lax.optimization_barrier((gathered_kv, states[-1]))
        piece = lax.dynamic_slice_in_dim(gathered_kv, first, window, 0)
        states.append(
            fold_piece(
                init, piece, query[head : head + 1], own_seg, own_start - first, key_seg, scale
            )
        )
    state = tuple(jnp.concatenate(parts, axis=0) for parts in zip(*states))
    attended = (state[2] / state[1][:, :, None]).astype(jnp.bfloat16)
    attended = jnp.transpose(attended, (1, 0, 2)).reshape(tok_dev, heads_dev * HEAD_SIZE)
    block_output = lax.psum_scatter(
        jnp.dot(attended, output_projection_weight, preferred_element_type=jnp.float32).astype(
            jnp.bfloat16
        ),
        ("row", "col"),
        scatter_dimension=0,
        tiled=True,
    )
    kv_cache = received.reshape(count_tok * capacity, heads_dev, 2, HEAD_SIZE)
    return (block_output, kv_cache)

def solution(mesh):
    placed = (
        P(("tok", "row"), "col"),
        P("col"),
        P("col", "row", None, None),
        P("col", None),
        P(None, "row", None, None),
        P(("row", "col"), None),
        P(),
        P("tok", None),
    )
    return jax.shard_map(
        shards_body,
        mesh=mesh,
        in_specs=placed,
        out_specs=(P(("tok", "row", "col"), None), P("tok", ("row", "col"), None, None)),
        check_vma=False,
    )
```

```python
import jax
import jax.numpy as jnp
from jax import lax
from jax.sharding import PartitionSpec as P


INPUT_WIDTH = 4096
HEAD_SIZE = 128
ADAPTER_RANK = 128
MAXLEN = 4352


def fold_piece(carry, piece, query, own_seg, own_start, prompt_segment_index, scale):
    top_old, _, _ = carry
    count = piece.shape[0]
    key_pos = jnp.arange(count, dtype=jnp.int32)
    query_pos = own_start + jnp.arange(query.shape[1], dtype=jnp.int32)
    allowed = (
        (own_seg[:, None] == prompt_segment_index[None, :])
        & (key_pos[None, :] <= query_pos[:, None])
        & (key_pos[None, :] >= 0)
    )
    score = (
        jnp.einsum("htd,shd->hts", query, piece[:, :, 0], preferred_element_type=jnp.float32)
        * scale
    )
    masked = jnp.where(allowed[None], score, -1e30)
    top_new = jnp.maximum(top_old, jnp.max(masked, axis=2))
    weights = jnp.where(allowed[None], jnp.exp(score - top_new[:, :, None]), 0.0).astype(
        jnp.bfloat16
    )
    total_new = jnp.sum(weights.astype(jnp.float32), axis=2)
    acc_new = jnp.einsum(
        "hts,shd->htd", weights, piece[:, :, 1], preferred_element_type=jnp.float32
    )
    return (top_new, total_new, acc_new)

def shards_body(
    block_input_rows,
    input_norm_scale,
    query_key_value_weight,
    adapter_down_weight,
    adapter_up_weight,
    output_projection_weight,
    prompt_segment_index,
    cache_owner_index,
):
    gathered = lax.all_gather(block_input_rows, "row", axis=0, tiled=True)
    wide = gathered.astype(jnp.float32)
    partial_sq = jnp.sum(wide * wide, axis=1)
    total_sq = lax.psum(partial_sq, "col")
    inverse = lax.rsqrt(total_sq / INPUT_WIDTH + 1e-06)
    normalized_input = (
        wide * inverse[:, None] * input_norm_scale.astype(jnp.float32)[None, :]
    ).astype(jnp.bfloat16)
    adapter_hidden = jnp.dot(
        normalized_input, adapter_down_weight, preferred_element_type=jnp.float32
    )
    tok_dev = gathered.shape[0]
    local_head_count = query_key_value_weight.shape[1]
    flat_weight = query_key_value_weight.reshape(
        query_key_value_weight.shape[0], local_head_count, 3 * HEAD_SIZE
    )
    flattened_up_weight = adapter_up_weight.reshape(ADAPTER_RANK, local_head_count, 3 * HEAD_SIZE)
    heads_dev = local_head_count // lax.axis_size("col")
    main = jnp.einsum(
        "td,dhe->hte", normalized_input, flat_weight, preferred_element_type=jnp.float32
    )
    adapter_down_output = jnp.einsum(
        "tr,rhe->hte",
        adapter_hidden,
        flattened_up_weight.astype(jnp.float32),
        precision=lax.Precision.HIGHEST,
    )
    mixed = lax.psum_scatter(main + adapter_down_output, "col", scatter_dimension=0, tiled=True)
    qkv = mixed.astype(jnp.bfloat16).reshape(heads_dev, tok_dev, 3, HEAD_SIZE)
    query = qkv[:, :, 0]
    kv_tok = jnp.transpose(qkv[:, :, 1:3], (1, 0, 2, 3))
    count_tok = lax.axis_size("tok")
    me = lax.axis_index("tok")
    own_start = me * tok_dev
    own_seg = lax.dynamic_slice_in_dim(prompt_segment_index, own_start, tok_dev, 0)
    scale = 1.0 / HEAD_SIZE**0.5
    back = min(count_tok - 1, -(-(MAXLEN - 1) // tok_dev))
    window = (back + 1) * tok_dev
    padded_seg = jnp.concatenate(
        [jnp.full((back * tok_dev,), -1, jnp.int32), prompt_segment_index]
    )
    key_seg = lax.dynamic_slice_in_dim(padded_seg, own_start, window, 0)
    init = (
        jnp.full((1, tok_dev), -1e30, jnp.float32),
        jnp.zeros((1, tok_dev), jnp.float32),
        jnp.zeros((1, tok_dev, HEAD_SIZE), jnp.float32),
    )
    capacity = max(2, 2 * tok_dev // count_tok)
    owner = cache_owner_index[:, 0]
    onehot = (owner[:, None] == jnp.arange(count_tok, dtype=jnp.int32)[None, :]).astype(jnp.int32)
    before = jnp.cumsum(onehot, axis=0) - onehot
    rank = jnp.sum(before * onehot, axis=1)
    slot = owner * capacity + rank
    selector = (jnp.arange(count_tok * capacity, dtype=jnp.int32)[:, None] == slot[None, :]).astype(
        jnp.bfloat16
    )
    outgoing = jnp.dot(
        selector,
        kv_tok.reshape(tok_dev, heads_dev * 2 * HEAD_SIZE),
        preferred_element_type=jnp.float32,
    ).astype(jnp.bfloat16).reshape(count_tok, capacity, heads_dev * 2 * HEAD_SIZE)
    blocks = [kv_tok]
    for shift in range(1, back + 1):
        pairs = [(j, j + shift) for j in range(count_tok - shift)]
        blocks.append(lax.ppermute(kv_tok, "tok", pairs))
    gathered_all = jnp.concatenate(blocks[::-1], axis=0)
    received = lax.all_to_all(outgoing, "tok", split_axis=0, concat_axis=0, tiled=True)
    received, gathered_all = lax.optimization_barrier((received, gathered_all))
    states = []
    for head in range(heads_dev):
        gathered_kv = gathered_all[:, head : head + 1]
        if head > 0:
            gathered_kv, _ = lax.optimization_barrier((gathered_kv, states[-1]))
        piece = gathered_kv
        states.append(
            fold_piece(init, piece, query[head : head + 1], own_seg, back * tok_dev, key_seg, scale)
        )
    state = tuple(jnp.concatenate(parts, axis=0) for parts in zip(*states))
    attended = (state[2] / state[1][:, :, None]).astype(jnp.bfloat16)
    attended = jnp.transpose(attended, (1, 0, 2)).reshape(tok_dev, heads_dev * HEAD_SIZE)
    block_output = lax.psum_scatter(
        jnp.dot(attended, output_projection_weight, preferred_element_type=jnp.float32).astype(
            jnp.bfloat16
        ),
        ("row", "col"),
        scatter_dimension=0,
        tiled=True,
    )
    kv_cache = received.reshape(count_tok * capacity, heads_dev, 2, HEAD_SIZE)
    return (block_output, kv_cache)

def solution(mesh):
    placed = (
        P(("tok", "row"), "col"),
        P("col"),
        P("col", "row", None, None),
        P("col", None),
        P(None, "row", None, None),
        P(("row", "col"), None),
        P(),
        P("tok", None),
    )
    return jax.shard_map(
        shards_body,
        mesh=mesh,
        in_specs=placed,
        out_specs=(P(("tok", "row", "col"), None), P("tok", ("row", "col"), None, None)),
        check_vma=False,
    )
```

```python
import jax
import jax.numpy as jnp
from jax import lax
from jax.sharding import PartitionSpec as P


INPUT_WIDTH = 4096
HEAD_SIZE = 128
ADAPTER_RANK = 128
MAXLEN = 4352

def fold_piece(carry, piece, query, own_seg, own_start, prompt_segment_index, scale):
    top_old, _, _ = carry
    count = piece.shape[0]
    key_pos = jnp.arange(count, dtype=jnp.int32)
    query_pos = own_start + jnp.arange(query.shape[1], dtype=jnp.int32)
    allowed = (
        (own_seg[:, None] == prompt_segment_index[None, :])
        & (key_pos[None, :] <= query_pos[:, None])
        & (key_pos[None, :] >= 0)
    )
    score = (
        jnp.einsum("htd,shd->hts", query, piece[:, :, 0], preferred_element_type=jnp.float32)
        * scale
    )
    masked = jnp.where(allowed[None], score, -1e30)
    top_new = jnp.maximum(top_old, jnp.max(masked, axis=2))
    weights = jnp.where(allowed[None], jnp.exp(score - top_new[:, :, None]), 0.0).astype(
        jnp.bfloat16
    )
    total_new = jnp.sum(weights.astype(jnp.float32), axis=2)
    acc_new = jnp.einsum(
        "hts,shd->htd", weights, piece[:, :, 1], preferred_element_type=jnp.float32
    )
    return (top_new, total_new, acc_new)

def shards_body(
    block_input_rows,
    input_norm_scale,
    query_key_value_weight,
    adapter_down_weight,
    adapter_up_weight,
    output_projection_weight,
    prompt_segment_index,
    cache_owner_index,
):
    gathered = lax.all_gather(block_input_rows, "row", axis=0, tiled=True)
    wide = gathered.astype(jnp.float32)
    partial_sq = jnp.sum(wide * wide, axis=1)
    total_sq = lax.psum(partial_sq, "col")
    inverse = lax.rsqrt(total_sq / INPUT_WIDTH + 1e-06)
    normalized_input = (
        wide * inverse[:, None] * input_norm_scale.astype(jnp.float32)[None, :]
    ).astype(jnp.bfloat16)
    adapter_hidden = jnp.dot(
        normalized_input, adapter_down_weight, preferred_element_type=jnp.float32
    )
    tok_dev = gathered.shape[0]
    local_head_count = query_key_value_weight.shape[1]
    flat_weight = query_key_value_weight.reshape(
        query_key_value_weight.shape[0], local_head_count, 3 * HEAD_SIZE
    )
    flattened_up_weight = adapter_up_weight.reshape(ADAPTER_RANK, local_head_count, 3 * HEAD_SIZE)
    heads_dev = local_head_count // lax.axis_size("col")
    main = jnp.einsum(
        "td,dhe->hte", normalized_input, flat_weight, preferred_element_type=jnp.float32
    )
    adapter_down_output = jnp.einsum(
        "tr,rhe->hte",
        adapter_hidden,
        flattened_up_weight.astype(jnp.float32),
        precision=lax.Precision.HIGHEST,
    )
    mixed = lax.psum_scatter(main + adapter_down_output, "col", scatter_dimension=0, tiled=True)
    qkv = mixed.astype(jnp.bfloat16).reshape(heads_dev, tok_dev, 3, HEAD_SIZE)
    query = qkv[:, :, 0]
    kv_tok = jnp.transpose(qkv[:, :, 1:3], (1, 0, 2, 3))
    count_tok = lax.axis_size("tok")
    me = lax.axis_index("tok")
    own_start = me * tok_dev
    own_seg = lax.dynamic_slice_in_dim(prompt_segment_index, own_start, tok_dev, 0)
    scale = 1.0 / HEAD_SIZE**0.5
    back = min(count_tok - 1, -(-(MAXLEN - 1) // tok_dev))
    window = (back + 1) * tok_dev
    first = jnp.clip(me - back, 0, count_tok - 1 - back) * tok_dev
    key_seg = lax.dynamic_slice_in_dim(prompt_segment_index, first, window, 0)
    init = (
        jnp.full((1, tok_dev), -1e30, jnp.float32),
        jnp.zeros((1, tok_dev), jnp.float32),
        jnp.zeros((1, tok_dev, HEAD_SIZE), jnp.float32),
    )
    capacity = max(2, 2 * tok_dev // count_tok)
    owner = cache_owner_index[:, 0]
    onehot = (owner[:, None] == jnp.arange(count_tok, dtype=jnp.int32)[None, :]).astype(jnp.int32)
    before = jnp.cumsum(onehot, axis=0) - onehot
    rank = jnp.sum(before * onehot, axis=1)
    slot = owner * capacity + rank
    selector = (jnp.arange(count_tok * capacity, dtype=jnp.int32)[:, None] == slot[None, :]).astype(
        jnp.bfloat16
    )
    outgoing = jnp.dot(
        selector,
        kv_tok.reshape(tok_dev, heads_dev * 2 * HEAD_SIZE),
        preferred_element_type=jnp.float32,
    ).astype(jnp.bfloat16).reshape(count_tok, capacity, heads_dev * 2 * HEAD_SIZE)
    gathered_all = lax.all_gather(kv_tok, "tok", axis=0, tiled=True)
    states = []
    for head in range(heads_dev):
        gathered_kv = gathered_all[:, head : head + 1]
        if head > 0:
            gathered_kv, _ = lax.optimization_barrier((gathered_kv, states[-1]))
        piece = lax.dynamic_slice_in_dim(gathered_kv, first, window, 0)
        states.append(
            fold_piece(
                init, piece, query[head : head + 1], own_seg, own_start - first, key_seg, scale
            )
        )
    state = tuple(jnp.concatenate(parts, axis=0) for parts in zip(*states))
    outgoing, _ = lax.optimization_barrier((outgoing, states[-1]))
    received = lax.all_to_all(outgoing, "tok", split_axis=0, concat_axis=0, tiled=True)
    attended = (state[2] / state[1][:, :, None]).astype(jnp.bfloat16)
    attended = jnp.transpose(attended, (1, 0, 2)).reshape(tok_dev, heads_dev * HEAD_SIZE)
    block_output = lax.psum_scatter(
        jnp.dot(attended, output_projection_weight, preferred_element_type=jnp.float32).astype(
            jnp.bfloat16
        ),
        ("row", "col"),
        scatter_dimension=0,
        tiled=True,
    )
    kv_cache = received.reshape(count_tok * capacity, heads_dev, 2, HEAD_SIZE)
    return (block_output, kv_cache)

def solution(mesh):
    placed = (
        P(("tok", "row"), "col"),
        P("col"),
        P("col", "row", None, None),
        P("col", None),
        P(None, "row", None, None),
        P(("row", "col"), None),
        P(),
        P("tok", None),
    )
    return jax.shard_map(
        shards_body,
        mesh=mesh,
        in_specs=placed,
        out_specs=(P(("tok", "row", "col"), None), P("tok", ("row", "col"), None, None)),
        check_vma=False,
    )
```

```python
import jax
import jax.numpy as jnp
from jax import lax
from jax.sharding import PartitionSpec as P


INPUT_WIDTH = 4096
HEAD_SIZE = 128
ADAPTER_RANK = 128
MAXLEN = 4352

def attend_head(query, keys, values, own_seg, own_start, key_seg, scale):
    count = keys.shape[0]
    key_pos = jnp.arange(count, dtype=jnp.int32)
    query_pos = own_start + jnp.arange(query.shape[0], dtype=jnp.int32)
    allowed = (own_seg[:, None] == key_seg[None, :]) & (key_pos[None, :] <= query_pos[:, None])
    score = jnp.dot(query, keys.T, preferred_element_type=jnp.float32) * scale
    masked = jnp.where(allowed, score, -1e30)
    top = jnp.max(masked, axis=1)
    weights = jnp.where(allowed, jnp.exp(score - top[:, None]), 0.0).astype(jnp.bfloat16)
    total = jnp.sum(weights.astype(jnp.float32), axis=1)
    summed = jnp.dot(weights, values, preferred_element_type=jnp.float32)
    return total, summed


def shards_body(
    block_input_rows,
    input_norm_scale,
    query_key_value_weight,
    adapter_down_weight,
    adapter_up_weight,
    output_projection_weight,
    prompt_segment_index,
    cache_owner_index,
):
    gathered = lax.all_gather(block_input_rows, "row", axis=0, tiled=True)
    wide = gathered.astype(jnp.float32)
    partial_sq = jnp.sum(wide * wide, axis=1)
    total_sq = lax.psum(partial_sq, "col")
    inverse = lax.rsqrt(total_sq / INPUT_WIDTH + 1e-06)
    normalized_input = (
        wide * inverse[:, None] * input_norm_scale.astype(jnp.float32)[None, :]
    ).astype(jnp.bfloat16)
    adapter_hidden = jnp.dot(
        normalized_input, adapter_down_weight, preferred_element_type=jnp.float32
    )
    tok_dev = gathered.shape[0]
    local_head_count = query_key_value_weight.shape[1]
    flat_weight = query_key_value_weight.reshape(
        query_key_value_weight.shape[0], local_head_count, 3 * HEAD_SIZE
    )
    flattened_up_weight = adapter_up_weight.reshape(ADAPTER_RANK, local_head_count, 3 * HEAD_SIZE)
    heads_dev = local_head_count // lax.axis_size("col")
    main = jnp.einsum(
        "td,dhe->hte", normalized_input, flat_weight, preferred_element_type=jnp.float32
    )
    adapter_down_output = jnp.einsum(
        "tr,rhe->hte",
        adapter_hidden,
        flattened_up_weight.astype(jnp.float32),
        precision=lax.Precision.HIGHEST,
    )
    mixed = lax.psum_scatter(main + adapter_down_output, "col", scatter_dimension=0, tiled=True)
    qkv = mixed.astype(jnp.bfloat16).reshape(heads_dev, tok_dev, 3, HEAD_SIZE)
    query = qkv[:, :, 0]
    kv_tok = jnp.transpose(qkv[:, :, 1:3], (1, 0, 2, 3))
    kv_flat = kv_tok.reshape(tok_dev, heads_dev * 2 * HEAD_SIZE)
    count_tok = lax.axis_size("tok")
    me = lax.axis_index("tok")
    own_start = me * tok_dev
    own_seg = lax.dynamic_slice_in_dim(prompt_segment_index, own_start, tok_dev, 0)
    scale = 1.0 / HEAD_SIZE**0.5
    back = min(count_tok - 1, -(-(MAXLEN - 1) // tok_dev))
    window = (back + 1) * tok_dev
    first = jnp.clip(me - back, 0, count_tok - 1 - back) * tok_dev
    key_seg = lax.dynamic_slice_in_dim(prompt_segment_index, first, window, 0)
    capacity = max(2, 2 * tok_dev // count_tok)
    owner = cache_owner_index[:, 0]
    onehot = (owner[:, None] == jnp.arange(count_tok, dtype=jnp.int32)[None, :]).astype(jnp.int32)
    before = jnp.cumsum(onehot, axis=0) - onehot
    rank = jnp.sum(before * onehot, axis=1)
    slot = owner * capacity + rank
    selector = (jnp.arange(count_tok * capacity, dtype=jnp.int32)[:, None] == slot[None, :]).astype(
        jnp.bfloat16
    )
    outgoing = jnp.dot(
        selector,
        kv_flat,
        preferred_element_type=jnp.float32,
    ).astype(jnp.bfloat16).reshape(count_tok, capacity, heads_dev * 2 * HEAD_SIZE)
    gathered_all = lax.all_gather(kv_flat, "tok", axis=0, tiled=True)
    window_kv = lax.dynamic_slice_in_dim(gathered_all, first, window, 0)
    states = []
    for head in range(heads_dev):
        head_kv = window_kv[:, head * 2 * HEAD_SIZE : (head + 1) * 2 * HEAD_SIZE]
        if head > 0:
            head_kv, _ = lax.optimization_barrier((head_kv, states[-1]))
        states.append(
            attend_head(
                query[head],
                head_kv[:, :HEAD_SIZE],
                head_kv[:, HEAD_SIZE:],
                own_seg,
                own_start - first,
                key_seg,
                scale,
            )
        )
    total = jnp.stack([part[0] for part in states])
    summed = jnp.stack([part[1] for part in states])
    outgoing, _ = lax.optimization_barrier((outgoing, states[-1]))
    received = lax.all_to_all(outgoing, "tok", split_axis=0, concat_axis=0, tiled=True)
    attended = (summed / total[:, :, None]).astype(jnp.bfloat16)
    attended = jnp.transpose(attended, (1, 0, 2)).reshape(tok_dev, heads_dev * HEAD_SIZE)
    block_output = lax.psum_scatter(
        jnp.dot(attended, output_projection_weight, preferred_element_type=jnp.float32).astype(
            jnp.bfloat16
        ),
        ("row", "col"),
        scatter_dimension=0,
        tiled=True,
    )
    kv_cache = received.reshape(count_tok * capacity, heads_dev, 2, HEAD_SIZE)
    return (block_output, kv_cache)

def solution(mesh):
    placed = (
        P(("tok", "row"), "col"),
        P("col"),
        P("col", "row", None, None),
        P("col", None),
        P(None, "row", None, None),
        P(("row", "col"), None),
        P(),
        P("tok", None),
    )
    return jax.shard_map(
        shards_body,
        mesh=mesh,
        in_specs=placed,
        out_specs=(P(("tok", "row", "col"), None), P("tok", ("row", "col"), None, None)),
        check_vma=False,
    )
```

```python
import functools

import jax
import jax.numpy as jnp
from jax import lax
from jax.experimental import pallas as pl
from jax.experimental.pallas import tpu as pltpu
from jax.sharding import PartitionSpec as P


INPUT_WIDTH = 4096
HEAD_SIZE = 128
ADAPTER_RANK = 128
MAXLEN = 4352

def attend_kernel(offset_ref, q_ref, k_ref, v_ref, qseg_ref, kseg_ref, o_ref, *, scale, rows):
    tile = pl.program_id(1)
    q = q_ref[0]
    k = k_ref[...]
    v = v_ref[...]
    count = k.shape[0]
    score = lax.dot_general(q, k, (((1,), (1,)), ((), ())), preferred_element_type=jnp.float32) * scale
    key_pos = lax.broadcasted_iota(jnp.int32, (rows, count), 1)
    query_pos = offset_ref[0] + tile * rows + lax.broadcasted_iota(jnp.int32, (rows, count), 0)
    allowed = (qseg_ref[...] == kseg_ref[...]) & (key_pos <= query_pos)
    masked = jnp.where(allowed, score, -1e30)
    top = jnp.max(masked, axis=1, keepdims=True)
    weights = jnp.where(allowed, jnp.exp(score - top), 0.0).astype(jnp.bfloat16)
    total = jnp.sum(weights.astype(jnp.float32), axis=1, keepdims=True)
    summed = jnp.dot(weights, v, preferred_element_type=jnp.float32)
    o_ref[0] = (summed / total).astype(o_ref.dtype)

def attend(query, window_kv, own_seg, key_seg, offset, scale, rows=128):
    heads, tokens, _ = query.shape
    count = window_kv.shape[0]
    grid = (heads, tokens // rows)
    kernel = functools.partial(attend_kernel, scale=scale, rows=rows)
    flops = 4 * heads * tokens * count * HEAD_SIZE
    return pl.pallas_call(
        kernel,
        out_shape=jax.ShapeDtypeStruct((heads, tokens, HEAD_SIZE), jnp.bfloat16),
        grid_spec=pltpu.PrefetchScalarGridSpec(
            num_scalar_prefetch=1,
            grid=grid,
            in_specs=[
                pl.BlockSpec((1, rows, HEAD_SIZE), lambda h, i, off: (h, i, 0)),
                pl.BlockSpec((count, HEAD_SIZE), lambda h, i, off: (0, 2 * h)),
                pl.BlockSpec((count, HEAD_SIZE), lambda h, i, off: (0, 2 * h + 1)),
                pl.BlockSpec((rows, 1), lambda h, i, off: (i, 0)),
                pl.BlockSpec((1, count), lambda h, i, off: (0, 0)),
            ],
            out_specs=pl.BlockSpec((1, rows, HEAD_SIZE), lambda h, i, off: (h, i, 0)),
        ),
        compiler_params=pltpu.CompilerParams(dimension_semantics=("arbitrary", "arbitrary"), vmem_limit_bytes=48 * 1024 * 1024),
        cost_estimate=pl.CostEstimate(flops=flops, transcendentals=heads * tokens * count, bytes_accessed=2 * count * 512 + 4 * heads * tokens * HEAD_SIZE),
    )(offset.reshape(1).astype(jnp.int32), query, window_kv, window_kv, own_seg.reshape(tokens, 1), key_seg.reshape(1, count))


def shards_body(
    block_input_rows,
    input_norm_scale,
    query_key_value_weight,
    adapter_down_weight,
    adapter_up_weight,
    output_projection_weight,
    prompt_segment_index,
    cache_owner_index,
):
    gathered = lax.all_gather(block_input_rows, "row", axis=0, tiled=True)
    wide = gathered.astype(jnp.float32)
    partial_sq = jnp.sum(wide * wide, axis=1)
    total_sq = lax.psum(partial_sq, "col")
    inverse = lax.rsqrt(total_sq / INPUT_WIDTH + 1e-06)
    normalized_input = (
        wide * inverse[:, None] * input_norm_scale.astype(jnp.float32)[None, :]
    ).astype(jnp.bfloat16)
    adapter_hidden = jnp.dot(
        normalized_input, adapter_down_weight, preferred_element_type=jnp.float32
    )
    tok_dev = gathered.shape[0]
    local_head_count = query_key_value_weight.shape[1]
    flat_weight = query_key_value_weight.reshape(
        query_key_value_weight.shape[0], local_head_count, 3 * HEAD_SIZE
    )
    flattened_up_weight = adapter_up_weight.reshape(ADAPTER_RANK, local_head_count, 3 * HEAD_SIZE)
    heads_dev = local_head_count // lax.axis_size("col")
    main = jnp.einsum(
        "td,dhe->hte", normalized_input, flat_weight, preferred_element_type=jnp.float32
    )
    adapter_down_output = jnp.einsum(
        "tr,rhe->hte",
        adapter_hidden,
        flattened_up_weight.astype(jnp.float32),
        precision=lax.Precision.HIGHEST,
    )
    mixed = lax.psum_scatter(main + adapter_down_output, "col", scatter_dimension=0, tiled=True)
    qkv = mixed.astype(jnp.bfloat16).reshape(heads_dev, tok_dev, 3, HEAD_SIZE)
    query = qkv[:, :, 0]
    kv_tok = jnp.transpose(qkv[:, :, 1:3], (1, 0, 2, 3))
    kv_flat = kv_tok.reshape(tok_dev, heads_dev * 2 * HEAD_SIZE)
    count_tok = lax.axis_size("tok")
    me = lax.axis_index("tok")
    own_start = me * tok_dev
    own_seg = lax.dynamic_slice_in_dim(prompt_segment_index, own_start, tok_dev, 0)
    scale = 1.0 / HEAD_SIZE**0.5
    back = min(count_tok - 1, -(-(MAXLEN - 1) // tok_dev))
    window = (back + 1) * tok_dev
    first = jnp.clip(me - back, 0, count_tok - 1 - back) * tok_dev
    key_seg = lax.dynamic_slice_in_dim(prompt_segment_index, first, window, 0)
    capacity = max(2, 2 * tok_dev // count_tok)
    owner = cache_owner_index[:, 0]
    onehot = (owner[:, None] == jnp.arange(count_tok, dtype=jnp.int32)[None, :]).astype(jnp.int32)
    before = jnp.cumsum(onehot, axis=0) - onehot
    rank = jnp.sum(before * onehot, axis=1)
    slot = owner * capacity + rank
    selector = (jnp.arange(count_tok * capacity, dtype=jnp.int32)[:, None] == slot[None, :]).astype(
        jnp.bfloat16
    )
    outgoing = jnp.dot(
        selector,
        kv_flat,
        preferred_element_type=jnp.float32,
    ).astype(jnp.bfloat16).reshape(count_tok, capacity, heads_dev * 2 * HEAD_SIZE)
    gathered_all = lax.all_gather(kv_flat, "tok", axis=0, tiled=True)
    window_kv = lax.dynamic_slice_in_dim(gathered_all, first, window, 0)
    attended = attend(query, window_kv, own_seg, key_seg, own_start - first, scale)
    outgoing, _ = lax.optimization_barrier((outgoing, attended))
    received = lax.all_to_all(outgoing, "tok", split_axis=0, concat_axis=0, tiled=True)
    attended = jnp.transpose(attended, (1, 0, 2)).reshape(tok_dev, heads_dev * HEAD_SIZE)
    block_output = lax.psum_scatter(
        jnp.dot(attended, output_projection_weight, preferred_element_type=jnp.float32).astype(
            jnp.bfloat16
        ),
        ("row", "col"),
        scatter_dimension=0,
        tiled=True,
    )
    kv_cache = received.reshape(count_tok * capacity, heads_dev, 2, HEAD_SIZE)
    return (block_output, kv_cache)

def solution(mesh):
    placed = (
        P(("tok", "row"), "col"),
        P("col"),
        P("col", "row", None, None),
        P("col", None),
        P(None, "row", None, None),
        P(("row", "col"), None),
        P(),
        P("tok", None),
    )
    return jax.shard_map(
        shards_body,
        mesh=mesh,
        in_specs=placed,
        out_specs=(P(("tok", "row", "col"), None), P("tok", ("row", "col"), None, None)),
        check_vma=False,
    )
```

```python
import functools

import jax
import jax.numpy as jnp
from jax import lax
from jax.experimental import pallas as pl
from jax.experimental.pallas import tpu as pltpu
from jax.sharding import PartitionSpec as P


INPUT_WIDTH = 4096
HEAD_SIZE = 128
ADAPTER_RANK = 128
MAXLEN = 4352
CHUNK = 512


def attend_kernel(off_ref, lo_ref, q_ref, k_ref, v_ref, low_ref, o_ref, *, scale, rows):
    tile = pl.program_id(1)
    q = q_ref[0]
    base = off_ref[0] + tile * rows
    query_pos = base + lax.broadcasted_iota(jnp.int32, (rows, 1), 0)
    low = low_ref[...]
    last_chunk = (base + rows - 1) // CHUNK
    first_chunk = jnp.clip(lo_ref[tile] // CHUNK, 0, last_chunk)

    def scores(chunk):
        start = pl.multiple_of(chunk * CHUNK, CHUNK)
        keys = k_ref[pl.ds(start, CHUNK), :]
        score = lax.dot_general(
            q, keys, (((1,), (1,)), ((), ())), preferred_element_type=jnp.float32
        ) * scale
        key_pos = start + lax.broadcasted_iota(jnp.int32, (rows, CHUNK), 1)
        allowed = (key_pos >= low) & (key_pos <= query_pos)
        return jnp.where(allowed, score, -1e30), start

    def top_step(chunk, top):
        masked, _ = scores(chunk)
        return jnp.maximum(top, jnp.max(masked, axis=1, keepdims=True))

    top = lax.fori_loop(
        first_chunk, last_chunk + 1, top_step, jnp.full((rows, 1), -1e30, jnp.float32)
    )

    def sum_step(chunk, carry):
        total, summed = carry
        masked, start = scores(chunk)
        weights = jnp.exp(masked - top).astype(jnp.bfloat16)
        total = total + jnp.sum(weights.astype(jnp.float32), axis=1, keepdims=True)
        values = v_ref[pl.ds(start, CHUNK), :]
        summed = summed + jnp.dot(weights, values, preferred_element_type=jnp.float32)
        return total, summed

    total, summed = lax.fori_loop(
        first_chunk,
        last_chunk + 1,
        sum_step,
        (jnp.zeros((rows, 1), jnp.float32), jnp.zeros((rows, HEAD_SIZE), jnp.float32)),
    )
    o_ref[0] = (summed / total).astype(o_ref.dtype)


def attend(query, window_kv, low, offset, scale, rows=128):
    heads, tokens, _ = query.shape
    count = window_kv.shape[0]
    tiles = tokens // rows
    kernel = functools.partial(attend_kernel, scale=scale, rows=rows)
    flops = 6 * heads * tokens * count * HEAD_SIZE
    tile_low = low.reshape(tiles, rows)[:, 0]
    return pl.pallas_call(
        kernel,
        out_shape=jax.ShapeDtypeStruct((heads, tokens, HEAD_SIZE), jnp.bfloat16),
        grid_spec=pltpu.PrefetchScalarGridSpec(
            num_scalar_prefetch=2,
            grid=(heads, tiles),
            in_specs=[
                pl.BlockSpec((1, rows, HEAD_SIZE), lambda h, i, off, lo: (h, i, 0)),
                pl.BlockSpec((count, HEAD_SIZE), lambda h, i, off, lo: (0, 2 * h)),
                pl.BlockSpec((count, HEAD_SIZE), lambda h, i, off, lo: (0, 2 * h + 1)),
                pl.BlockSpec((rows, 1), lambda h, i, off, lo: (i, 0)),
            ],
            out_specs=pl.BlockSpec((1, rows, HEAD_SIZE), lambda h, i, off, lo: (h, i, 0)),
        ),
        compiler_params=pltpu.CompilerParams(
            dimension_semantics=("arbitrary", "arbitrary"), vmem_limit_bytes=48 * 1024 * 1024
        ),
        cost_estimate=pl.CostEstimate(
            flops=flops,
            transcendentals=heads * tokens * count,
            bytes_accessed=2 * count * 512 + 4 * heads * tokens * HEAD_SIZE,
        ),
    )(offset.reshape(1).astype(jnp.int32), tile_low, query, window_kv, window_kv, low.reshape(tokens, 1))


def shards_body(
    block_input_rows,
    input_norm_scale,
    query_key_value_weight,
    adapter_down_weight,
    adapter_up_weight,
    output_projection_weight,
    prompt_segment_index,
    cache_owner_index,
):
    gathered = lax.all_gather(block_input_rows, "row", axis=0, tiled=True)
    wide = gathered.astype(jnp.float32)
    partial_sq = jnp.sum(wide * wide, axis=1)
    total_sq = lax.psum(partial_sq, "col")
    inverse = lax.rsqrt(total_sq / INPUT_WIDTH + 1e-06)
    normalized_input = (
        wide * inverse[:, None] * input_norm_scale.astype(jnp.float32)[None, :]
    ).astype(jnp.bfloat16)
    adapter_hidden = jnp.dot(
        normalized_input, adapter_down_weight, preferred_element_type=jnp.float32
    )
    tok_dev = gathered.shape[0]
    local_head_count = query_key_value_weight.shape[1]
    flat_weight = query_key_value_weight.reshape(
        query_key_value_weight.shape[0], local_head_count, 3 * HEAD_SIZE
    )
    flattened_up_weight = adapter_up_weight.reshape(ADAPTER_RANK, local_head_count, 3 * HEAD_SIZE)
    heads_dev = local_head_count // lax.axis_size("col")
    main = jnp.einsum(
        "td,dhe->hte", normalized_input, flat_weight, preferred_element_type=jnp.float32
    )
    adapter_down_output = jnp.einsum(
        "tr,rhe->hte",
        adapter_hidden,
        flattened_up_weight.astype(jnp.float32),
        precision=lax.Precision.HIGHEST,
    )
    mixed = lax.psum_scatter(main + adapter_down_output, "col", scatter_dimension=0, tiled=True)
    qkv = mixed.astype(jnp.bfloat16).reshape(heads_dev, tok_dev, 3, HEAD_SIZE)
    query = qkv[:, :, 0]
    kv_tok = jnp.transpose(qkv[:, :, 1:3], (1, 0, 2, 3))
    kv_flat = kv_tok.reshape(tok_dev, heads_dev * 2 * HEAD_SIZE)
    count_tok = lax.axis_size("tok")
    me = lax.axis_index("tok")
    own_start = me * tok_dev
    own_seg = lax.dynamic_slice_in_dim(prompt_segment_index, own_start, tok_dev, 0)
    scale = 1.0 / HEAD_SIZE**0.5
    back = min(count_tok - 1, -(-(MAXLEN - 1) // tok_dev))
    window = (back + 1) * tok_dev
    first = jnp.clip(me - back, 0, count_tok - 1 - back) * tok_dev
    capacity = max(2, 2 * tok_dev // count_tok)
    owner = cache_owner_index[:, 0]
    onehot = (owner[:, None] == jnp.arange(count_tok, dtype=jnp.int32)[None, :]).astype(jnp.int32)
    before = jnp.cumsum(onehot, axis=0) - onehot
    rank = jnp.sum(before * onehot, axis=1)
    slot = owner * capacity + rank
    selector = (jnp.arange(count_tok * capacity, dtype=jnp.int32)[:, None] == slot[None, :]).astype(
        jnp.bfloat16
    )
    outgoing = jnp.dot(
        selector,
        kv_flat,
        preferred_element_type=jnp.float32,
    ).astype(jnp.bfloat16).reshape(count_tok, capacity, heads_dev * 2 * HEAD_SIZE)
    gathered_all = lax.all_gather(kv_flat, "tok", axis=0, tiled=True)
    window_kv = lax.dynamic_slice_in_dim(gathered_all, first, window, 0)
    seg_start = jnp.searchsorted(
        prompt_segment_index, own_seg, side="left", method="scan_unrolled"
    ).astype(jnp.int32)
    attended = attend(query, window_kv, seg_start - first, own_start - first, scale)
    outgoing, _ = lax.optimization_barrier((outgoing, attended))
    received = lax.all_to_all(outgoing, "tok", split_axis=0, concat_axis=0, tiled=True)
    attended = jnp.transpose(attended, (1, 0, 2)).reshape(tok_dev, heads_dev * HEAD_SIZE)
    block_output = lax.psum_scatter(
        jnp.dot(attended, output_projection_weight, preferred_element_type=jnp.float32).astype(
            jnp.bfloat16
        ),
        ("row", "col"),
        scatter_dimension=0,
        tiled=True,
    )
    kv_cache = received.reshape(count_tok * capacity, heads_dev, 2, HEAD_SIZE)
    return (block_output, kv_cache)


def solution(mesh):
    placed = (
        P(("tok", "row"), "col"),
        P("col"),
        P("col", "row", None, None),
        P("col", None),
        P(None, "row", None, None),
        P(("row", "col"), None),
        P(),
        P("tok", None),
    )
    return jax.shard_map(
        shards_body,
        mesh=mesh,
        in_specs=placed,
        out_specs=(P(("tok", "row", "col"), None), P("tok", ("row", "col"), None, None)),
        check_vma=False,
    )
```

```python
import functools

import jax
import jax.numpy as jnp
from jax import lax
from jax.experimental import pallas as pl
from jax.experimental.pallas import tpu as pltpu
from jax.sharding import PartitionSpec as P


INPUT_WIDTH = 4096
HEAD_SIZE = 128
ADAPTER_RANK = 128
MAXLEN = 4352


def attend_kernel(offset_ref, q_ref, k_ref, v_ref, low_ref, o_ref, *, scale, rows):
    tile = pl.program_id(1)
    q = q_ref[0]
    k = k_ref[...]
    v = v_ref[...]
    count = k.shape[0]
    score = lax.dot_general(
        q, k, (((1,), (1,)), ((), ())), preferred_element_type=jnp.float32
    ) * scale
    key_pos = lax.broadcasted_iota(jnp.int32, (rows, count), 1)
    query_pos = offset_ref[0] + tile * rows + lax.broadcasted_iota(jnp.int32, (rows, 1), 0)
    allowed = (key_pos >= low_ref[...]) & (key_pos <= query_pos)
    masked = jnp.where(allowed, score, -1e30)
    top = jnp.max(masked, axis=1, keepdims=True)
    weights = jnp.exp(masked - top).astype(jnp.bfloat16)
    total = jnp.sum(weights.astype(jnp.float32), axis=1, keepdims=True)
    summed = jnp.dot(weights, v, preferred_element_type=jnp.float32)
    o_ref[0] = (summed / total).astype(o_ref.dtype)


def attend(query, window_kv, low, offset, scale, rows=256):
    heads, tokens, _ = query.shape
    count = window_kv.shape[0]
    grid = (heads, tokens // rows)
    kernel = functools.partial(attend_kernel, scale=scale, rows=rows)
    flops = 4 * heads * tokens * count * HEAD_SIZE
    return pl.pallas_call(
        kernel,
        out_shape=jax.ShapeDtypeStruct((heads, tokens, HEAD_SIZE), jnp.bfloat16),
        grid_spec=pltpu.PrefetchScalarGridSpec(
            num_scalar_prefetch=1,
            grid=grid,
            in_specs=[
                pl.BlockSpec((1, rows, HEAD_SIZE), lambda h, i, off: (h, i, 0)),
                pl.BlockSpec((count, HEAD_SIZE), lambda h, i, off: (0, 2 * h)),
                pl.BlockSpec((count, HEAD_SIZE), lambda h, i, off: (0, 2 * h + 1)),
                pl.BlockSpec((rows, 1), lambda h, i, off: (i, 0)),
            ],
            out_specs=pl.BlockSpec((1, rows, HEAD_SIZE), lambda h, i, off: (h, i, 0)),
        ),
        compiler_params=pltpu.CompilerParams(
            dimension_semantics=("arbitrary", "arbitrary"), vmem_limit_bytes=56 * 1024 * 1024
        ),
        cost_estimate=pl.CostEstimate(
            flops=flops,
            transcendentals=heads * tokens * count,
            bytes_accessed=2 * count * 512 + 4 * heads * tokens * HEAD_SIZE,
        ),
    )(offset.reshape(1).astype(jnp.int32), query, window_kv, window_kv, low.reshape(tokens, 1))


def shards_body(
    block_input_rows,
    input_norm_scale,
    query_key_value_weight,
    adapter_down_weight,
    adapter_up_weight,
    output_projection_weight,
    prompt_segment_index,
    cache_owner_index,
):
    gathered = lax.all_gather(block_input_rows, "row", axis=0, tiled=True)
    wide = gathered.astype(jnp.float32)
    partial_sq = jnp.sum(wide * wide, axis=1)
    total_sq = lax.psum(partial_sq, "col")
    inverse = lax.rsqrt(total_sq / INPUT_WIDTH + 1e-06)
    normalized_input = (
        wide * inverse[:, None] * input_norm_scale.astype(jnp.float32)[None, :]
    ).astype(jnp.bfloat16)
    adapter_hidden = jnp.dot(
        normalized_input, adapter_down_weight, preferred_element_type=jnp.float32
    )
    tok_dev = gathered.shape[0]
    local_head_count = query_key_value_weight.shape[1]
    flat_weight = query_key_value_weight.reshape(
        query_key_value_weight.shape[0], local_head_count, 3 * HEAD_SIZE
    )
    flattened_up_weight = adapter_up_weight.reshape(ADAPTER_RANK, local_head_count, 3 * HEAD_SIZE)
    heads_dev = local_head_count // lax.axis_size("col")
    main = jnp.einsum(
        "td,dhe->hte", normalized_input, flat_weight, preferred_element_type=jnp.float32
    )
    adapter_down_output = jnp.einsum(
        "tr,rhe->hte",
        adapter_hidden,
        flattened_up_weight.astype(jnp.float32),
        precision=lax.Precision.HIGHEST,
    )
    mixed = lax.psum_scatter(main + adapter_down_output, "col", scatter_dimension=0, tiled=True)
    qkv = mixed.astype(jnp.bfloat16).reshape(heads_dev, tok_dev, 3, HEAD_SIZE)
    query = qkv[:, :, 0]
    kv_tok = jnp.transpose(qkv[:, :, 1:3], (1, 0, 2, 3))
    kv_flat = kv_tok.reshape(tok_dev, heads_dev * 2 * HEAD_SIZE)
    count_tok = lax.axis_size("tok")
    me = lax.axis_index("tok")
    own_start = me * tok_dev
    own_seg = lax.dynamic_slice_in_dim(prompt_segment_index, own_start, tok_dev, 0)
    scale = 1.0 / HEAD_SIZE**0.5
    back = min(count_tok - 1, -(-(MAXLEN - 1) // tok_dev))
    window = (back + 1) * tok_dev
    first = jnp.clip(me - back, 0, count_tok - 1 - back) * tok_dev
    capacity = max(2, 2 * tok_dev // count_tok)
    owner = cache_owner_index[:, 0]
    onehot = (owner[:, None] == jnp.arange(count_tok, dtype=jnp.int32)[None, :]).astype(jnp.int32)
    before = jnp.cumsum(onehot, axis=0) - onehot
    rank = jnp.sum(before * onehot, axis=1)
    slot = owner * capacity + rank
    selector = (jnp.arange(count_tok * capacity, dtype=jnp.int32)[:, None] == slot[None, :]).astype(
        jnp.bfloat16
    )
    outgoing = jnp.dot(
        selector,
        kv_flat,
        preferred_element_type=jnp.float32,
    ).astype(jnp.bfloat16).reshape(count_tok, capacity, heads_dev * 2 * HEAD_SIZE)
    gathered_all = lax.all_gather(kv_flat, "tok", axis=0, tiled=True)
    window_kv = lax.dynamic_slice_in_dim(gathered_all, first, window, 0)
    seg_start = jnp.sum(
        (prompt_segment_index[None, :] < own_seg[:, None]).astype(jnp.int32), axis=1
    )
    attended = attend(query, window_kv, seg_start - first, own_start - first, scale)
    outgoing, _ = lax.optimization_barrier((outgoing, attended))
    received = lax.all_to_all(outgoing, "tok", split_axis=0, concat_axis=0, tiled=True)
    attended = jnp.transpose(attended, (1, 0, 2)).reshape(tok_dev, heads_dev * HEAD_SIZE)
    block_output = lax.psum_scatter(
        jnp.dot(attended, output_projection_weight, preferred_element_type=jnp.float32).astype(
            jnp.bfloat16
        ),
        ("row", "col"),
        scatter_dimension=0,
        tiled=True,
    )
    kv_cache = received.reshape(count_tok * capacity, heads_dev, 2, HEAD_SIZE)
    return (block_output, kv_cache)


def solution(mesh):
    placed = (
        P(("tok", "row"), "col"),
        P("col"),
        P("col", "row", None, None),
        P("col", None),
        P(None, "row", None, None),
        P(("row", "col"), None),
        P(),
        P("tok", None),
    )
    return jax.shard_map(
        shards_body,
        mesh=mesh,
        in_specs=placed,
        out_specs=(P(("tok", "row", "col"), None), P("tok", ("row", "col"), None, None)),
        check_vma=False,
    )
```
